32 devices in a mesh: group: 2 (over y), cell: 8 (over z, x), head: 2 (over core).
Axes of the slice: x: 2, y: 2, z: 4, core: 2. Of those that a mesh axis runs over, the one named last changes fastest.
Arguments:
- latents: bfloat16 [4096, 1024], P(('group', 'cell')), parts along dimension 0, may hold values from -6.2 to 6.2
- cells: bfloat16 [16384, 1024], P(('group', 'cell')), parts along dimension 0, may hold values from -6 to 6
- w_query: bfloat16 [1024, 1024], P(None, 'head'), may hold values from -1.53125 to 1.53125
- w_key: bfloat16 [1024, 1024], P(None, 'head'), may hold values from -0.134375 to 0.134375
- w_value: bfloat16 [1024, 1024], P(None, 'head'), may hold values from -0.1875 to 0.1875
- w_out: bfloat16 [1024, 1024], replicated, may hold values from -0.1875 to 0.1875
- w_up: bfloat16 [1024, 4096], P(None, ('cell', 'head')), may hold values from -0.1875 to 0.1875
- w_down: bfloat16 [4096, 1024], P(('cell', 'head')), may hold values from -0.09375 to 0.09375
Outputs:
- prototypes: bfloat16 [4096, 1024], P(('group', 'cell', 'head')), parts along dimension 0
The draws below stay inside these ranges and needn't reach their ends.
There are 2 independent parts, one for each index of `group`. The reference program is written for one: setup_inputs(seed, part) draws one part's arguments, and reference() takes and returns one part's arrays. A program takes and returns all parts, laid end to end along the dimension named above; an argument that names none is the same for every part. Nothing has to cross between parts.
All inputs are finite; a program needn't handle non-finite values.
Results may differ from the reference program's by a relative error of at most 0.015.
Values may be sent and summed in bfloat16 or wider, within the bound.
No kernel may reach another device: no remote copies, remote signals or barrier semaphores. Data moves between devices by JAX's collectives and lax.ppermute only.
A program may use at most 128 MiB of HBM per device.

```python
import jax
import jax.numpy as jnp
from jax import lax

D = 1024
HEADS = 16
HEAD_DIM = 64
LAT = 2048
FF = 4096
CELL_DEV = 1024
CELLS = 8192
N_CELL = 8


def draw_cells(key, part):
    return jnp.clip(jax.random.normal(jax.random.fold_in(key, 205), (CELLS, D), jnp.float32), -6.0, 6.0).astype(jnp.bfloat16)


def draw_latents(key, part):
    return jnp.clip(jax.random.normal(jax.random.fold_in(key, 207), (LAT, D), jnp.float32), -6.0, 6.0).astype(jnp.bfloat16)


def draw_w_query(key, part):
    return (3.0 * D ** (-0.5) * jnp.clip(jax.random.normal(jax.random.fold_in(key, 302), (D, D), jnp.float32), -4.0, 4.0)).astype(jnp.bfloat16)


def draw_w_key(key, part):
    return (D ** (-0.5) * jnp.clip(jax.random.normal(jax.random.fold_in(key, 304), (D, D), jnp.float32), -4.0, 4.0)).astype(jnp.bfloat16)


def block_levels(stream_key, shape, shards, smallest, high):
    def one(position, blocks):
        heights = jax.random.uniform(jax.random.fold_in(jax.random.fold_in(stream_key, 6), position), (blocks,), jnp.float32, smallest / len(shards), high / len(shards))
        return jnp.repeat(jnp.exp(heights), shape[position] // blocks).reshape((-1,) + (1,) * (len(shape) - position - 1))

    gain = one(*shards[0])
    for cut in shards[1:]:
        gain = gain * one(*cut)
    return gain


def normal_values(rng, extent, deviation, bound, cuts=(), kind=jnp.bfloat16):
    array = jax.random.normal(rng, extent, jnp.float32) * deviation
    if len(cuts) > 0:
        array = block_levels(rng, extent, cuts, -0.22, 0.18) * array
    return jnp.clip(array, min=-bound, max=bound).astype(kind)


def setup_inputs(seed: int = 0, part: int = 0) -> dict:
    splits = jax.random.split(jax.random.key(seed), 9)
    own_keys = jax.random.split(jax.random.fold_in(splits[8], part), 9)
    latents = draw_latents(jax.random.fold_in(jax.random.fold_in(splits[8], part), 71), part)
    cells = draw_cells(jax.random.fold_in(jax.random.fold_in(splits[8], part), 71), part)
    w_query = draw_w_query(jax.random.fold_in(splits[8], 71), part)
    w_key = draw_w_key(jax.random.fold_in(splits[8], 71), part)
    w_value = normal_values(splits[4], (D, D), D ** -0.5, 0.1875, ((1, 2),))
    w_out = normal_values(splits[5], (D, D), D ** -0.5, 0.1875)
    w_up = normal_values(splits[6], (D, FF), D ** -0.5, 0.1875, ((1, 16),))
    w_down = normal_values(splits[7], (FF, D), FF ** -0.5, 0.09375, ((0, 16),))
    return {"latents": latents, "cells": cells, "w_query": w_query, "w_key": w_key, "w_value": w_value, "w_out": w_out, "w_up": w_up, "w_down": w_down}


def reference(latents, cells, w_query, w_key, w_value, w_out, w_up, w_down):
    queries = jnp.dot(latents, w_query, preferred_element_type=jnp.float32).astype(jnp.bfloat16)
    key_rows = jnp.dot(cells, w_key, preferred_element_type=jnp.float32).astype(jnp.bfloat16)
    value_rows = jnp.dot(cells, w_value, preferred_element_type=jnp.float32).astype(jnp.bfloat16)
    factor = HEAD_DIM ** (-0.5)
    query_heads = jnp.transpose(queries.reshape(LAT, HEADS, HEAD_DIM), (1, 0, 2)).astype(jnp.float32)

    def one_block(carry, block_index):
        old_max, old_tot, old_sum = carry
        start = (block_index * CELL_DEV).astype(jnp.int32)
        key_block = lax.dynamic_slice_in_dim(key_rows, start, CELL_DEV, 0).reshape(CELL_DEV, HEADS, HEAD_DIM).astype(jnp.float32)
        value_block = lax.dynamic_slice_in_dim(value_rows, start, CELL_DEV, 0).reshape(CELL_DEV, HEADS, HEAD_DIM).astype(jnp.float32)
        scores = jnp.einsum('hld,chd->hlc', query_heads, key_block) * factor
        block_max = lax.optimization_barrier(jnp.max(scores, axis=2))
        weights = jnp.exp(scores - block_max[:, :, None])
        block_tot = lax.optimization_barrier(jnp.sum(weights, axis=2))
        rounded = lax.optimization_barrier(weights.astype(jnp.bfloat16))
        block_sum = jnp.einsum('hlc,chd->hld', rounded.astype(jnp.float32), value_block)
        new_max = jnp.maximum(old_max, block_max)
        keep = jnp.exp(old_max - new_max)
        fresh = jnp.exp(block_max - new_max)
        new_tot = old_tot * keep + block_tot * fresh
        new_sum = old_sum * keep[:, :, None] + block_sum * fresh[:, :, None]
        return ((new_max, new_tot, new_sum), None)
    start_carry = (jnp.full((HEADS, LAT), -1e+30, jnp.float32), jnp.zeros((HEADS, LAT), jnp.float32), jnp.zeros((HEADS, LAT, HEAD_DIM), jnp.float32))
    final, unused = lax.scan(one_block, start_carry, jnp.arange(N_CELL, dtype=jnp.int32))
    maxima, totals, summed = final
    attended = (summed / totals[:, :, None]).astype(jnp.bfloat16)
    attended = jnp.transpose(attended, (1, 0, 2)).reshape(LAT, D)
    updated = (latents.astype(jnp.float32) + jnp.dot(attended, w_out, preferred_element_type=jnp.float32)).astype(jnp.bfloat16)
    widened = updated.astype(jnp.float32)
    normed = (widened * lax.rsqrt(lax.optimization_barrier(jnp.mean(widened * widened, axis=1, keepdims=True)) + 1e-05)).astype(jnp.bfloat16)
    hidden = jax.nn.gelu(jnp.dot(normed, w_up, preferred_element_type=jnp.float32), approximate=True).astype(jnp.bfloat16)
    return (widened + jnp.dot(hidden, w_down, preferred_element_type=jnp.float32)).astype(jnp.bfloat16)
```

```python
import functools

import jax
import jax.numpy as jnp
from jax import lax
from jax.experimental import pallas as pl
from jax.experimental.pallas import tpu as pltpu
from jax.sharding import PartitionSpec as P

HEAD_DIM = 64
LAT_TILE = 512


def attention_kernel(q_ref, k_ref, vt_ref, o_ref, ml_ref):
    factor = HEAD_DIM ** (-0.5)
    for j in range(2):
        cols = slice(j * HEAD_DIM, (j + 1) * HEAD_DIM)
        q = q_ref[:, cols]
        k = k_ref[:, cols]
        scores = (
            lax.dot_general(k, q, (((1,), (1,)), ((), ())), preferred_element_type=jnp.float32)
            * factor
        )
        block_max = jnp.max(scores, axis=0, keepdims=True)
        weights = jnp.exp(scores - block_max)
        block_tot = jnp.sum(weights, axis=0, keepdims=True)
        summed = jnp.dot(
            vt_ref[cols, :], weights.astype(jnp.bfloat16), preferred_element_type=jnp.float32
        )
        o_ref[cols, :] = summed
        ml_ref[0, j : j + 1, :] = block_max
        ml_ref[1, j : j + 1, :] = block_tot


def block_attention(queries, key_rows, value_t):
    lat, width = queries.shape
    cells = key_rows.shape[0]
    pairs = width // (2 * HEAD_DIM)
    tile = min(LAT_TILE, lat)
    return pl.pallas_call(
        attention_kernel,
        grid=(pairs, lat // tile),
        in_specs=[
            pl.BlockSpec((tile, 2 * HEAD_DIM), lambda p, i: (i, p)),
            pl.BlockSpec((cells, 2 * HEAD_DIM), lambda p, i: (0, p)),
            pl.BlockSpec((2 * HEAD_DIM, cells), lambda p, i: (p, 0)),
        ],
        out_specs=[
            pl.BlockSpec((2 * HEAD_DIM, tile), lambda p, i: (p, i)),
            pl.BlockSpec((2, None, 2, tile), lambda p, i: (0, p, 0, i)),
        ],
        out_shape=[
            jax.ShapeDtypeStruct((width, lat), jnp.float32),
            jax.ShapeDtypeStruct((2, pairs, 2, lat), jnp.float32),
        ],
    )(queries, key_rows, value_t)


def body(latents, cells, w_query, w_key, w_value, w_out, w_up, w_down):
    key_rows = jnp.dot(cells, w_key, preferred_element_type=jnp.float32).astype(jnp.bfloat16)
    value_t = jnp.dot(cells, w_value, preferred_element_type=jnp.float32).astype(jnp.bfloat16).T
    local_queries = jnp.dot(latents, w_query, preferred_element_type=jnp.float32).astype(
        jnp.bfloat16
    )
    queries = lax.all_gather(local_queries, "cell", axis=0, tiled=True)
    lat, width = queries.shape
    heads_local = width // HEAD_DIM
    n_cell = lax.axis_size("cell")
    n_head = lax.axis_size("head")
    owners = n_cell * n_head
    rows = lat // owners

    sums_t, ml = block_attention(queries, key_rows, value_t)
    ml = ml.reshape(2 * heads_local, lat)
    sums_recv = lax.all_to_all(
        sums_t.astype(jnp.bfloat16), ("cell", "head"), split_axis=1, concat_axis=0, tiled=True
    )
    ml_recv = lax.all_to_all(ml, ("cell", "head"), split_axis=1, concat_axis=0, tiled=True)
    sums_recv = sums_recv.reshape(n_cell, n_head, heads_local, HEAD_DIM, rows).astype(jnp.float32)
    ml_recv = ml_recv.reshape(n_cell, n_head, 2, heads_local, rows)
    block_max = ml_recv[:, :, 0]
    block_tot = ml_recv[:, :, 1]
    maxima = jnp.max(block_max, axis=0)
    shrink = jnp.exp(block_max - maxima[None])
    totals = jnp.sum(shrink * block_tot, axis=0)
    summed = jnp.sum(shrink[:, :, :, None, :] * sums_recv, axis=0)
    attended_t = summed / totals[:, :, None, :]
    attended = attended_t.reshape(n_head * width, rows).T.astype(jnp.bfloat16)

    own_index = lax.axis_index("cell") * n_head + lax.axis_index("head")
    local_rows = latents.shape[0]
    own_latents = lax.dynamic_slice_in_dim(
        latents, (own_index % (local_rows // rows)) * rows, rows, 0
    )
    projected = jnp.dot(attended, w_out, preferred_element_type=jnp.float32)
    updated = (own_latents.astype(jnp.float32) + projected).astype(jnp.bfloat16)
    widened = updated.astype(jnp.float32)
    normed = (
        widened * lax.rsqrt(jnp.mean(widened * widened, axis=1, keepdims=True) + 1e-05)
    ).astype(jnp.bfloat16)
    hidden = jax.nn.gelu(
        jnp.dot(
            normed,
            lax.all_gather(w_up, ("cell", "head"), axis=1, tiled=True),
            preferred_element_type=jnp.float32,
        ),
        approximate=True,
    ).astype(jnp.bfloat16)
    mlp_out = jnp.dot(
        hidden,
        lax.all_gather(w_down, ("cell", "head"), axis=0, tiled=True),
        preferred_element_type=jnp.float32,
    )
    return (widened + mlp_out).astype(jnp.bfloat16)


def solution(mesh):
    return jax.shard_map(
        body,
        mesh=mesh,
        in_specs=(
            P(("group", "cell"), None),
            P(("group", "cell"), None),
            P(None, "head"),
            P(None, "head"),
            P(None, "head"),
            P(),
            P(None, ("cell", "head")),
            P(("cell", "head"), None),
        ),
        out_specs=P(("group", "cell", "head"), None),
        check_vma=False,
    )
```

```python
import functools

import jax
import jax.numpy as jnp
from jax import lax
from jax.experimental import pallas as pl
from jax.experimental.pallas import tpu as pltpu
from jax.sharding import PartitionSpec as P

HEAD_DIM = 64
LAT_TILE = 512


def attention_kernel(q_ref, k_ref, vt_ref, o_ref, ml_ref):
    factor = HEAD_DIM ** (-0.5)
    for j in range(2):
        cols = slice(j * HEAD_DIM, (j + 1) * HEAD_DIM)
        q = q_ref[:, cols]
        k = k_ref[:, cols]
        scores = (
            lax.dot_general(k, q, (((1,), (1,)), ((), ())), preferred_element_type=jnp.float32)
            * factor
        )
        block_max = jnp.max(scores, axis=0, keepdims=True)
        weights = jnp.exp(scores - block_max)
        block_tot = jnp.sum(weights, axis=0, keepdims=True)
        summed = jnp.dot(
            vt_ref[cols, :], weights.astype(jnp.bfloat16), preferred_element_type=jnp.float32
        )
        o_ref[cols, :] = summed
        ml_ref[0, j : j + 1, :] = block_max
        ml_ref[1, j : j + 1, :] = block_tot


def block_attention(queries, key_rows, value_t):
    lat, width = queries.shape
    cells = key_rows.shape[0]
    pairs = width // (2 * HEAD_DIM)
    tile = min(LAT_TILE, lat)
    return pl.pallas_call(
        attention_kernel,
        grid=(pairs, lat // tile),
        in_specs=[
            pl.BlockSpec((tile, 2 * HEAD_DIM), lambda p, i: (i, p)),
            pl.BlockSpec((cells, 2 * HEAD_DIM), lambda p, i: (0, p)),
            pl.BlockSpec((2 * HEAD_DIM, cells), lambda p, i: (p, 0)),
        ],
        out_specs=[
            pl.BlockSpec((2 * HEAD_DIM, tile), lambda p, i: (p, i)),
            pl.BlockSpec((2, None, 2, tile), lambda p, i: (0, p, 0, i)),
        ],
        out_shape=[
            jax.ShapeDtypeStruct((width, lat), jnp.float32),
            jax.ShapeDtypeStruct((2, pairs, 2, lat), jnp.float32),
        ],
    )(queries, key_rows, value_t)


def body(latents, cells, w_query, w_key, w_value, w_out, w_up, w_down):
    key_rows = jnp.dot(cells, w_key, preferred_element_type=jnp.float32).astype(jnp.bfloat16)
    value_t = jnp.dot(cells, w_value, preferred_element_type=jnp.float32).astype(jnp.bfloat16).T
    local_queries = jnp.dot(latents, w_query, preferred_element_type=jnp.float32).astype(
        jnp.bfloat16
    )
    queries = lax.all_gather(local_queries, "cell", axis=0, tiled=True)
    lat, width = queries.shape
    heads_local = width // HEAD_DIM
    n_cell = lax.axis_size("cell")
    n_head = lax.axis_size("head")
    owners = n_cell * n_head
    rows = lat // owners

    sums_t, ml = block_attention(queries, key_rows, value_t)
    ml = ml.reshape(2 * heads_local, lat)
    sums_recv = lax.all_to_all(
        sums_t.astype(jnp.bfloat16), ("cell", "head"), split_axis=1, concat_axis=0, tiled=True
    )
    ml_recv = lax.all_to_all(ml, ("cell", "head"), split_axis=1, concat_axis=0, tiled=True)
    sums_recv = sums_recv.reshape(n_cell, n_head, heads_local, HEAD_DIM, rows).astype(jnp.float32)
    ml_recv = ml_recv.reshape(n_cell, n_head, 2, heads_local, rows)
    block_max = ml_recv[:, :, 0]
    block_tot = ml_recv[:, :, 1]
    maxima = jnp.max(block_max, axis=0)
    shrink = jnp.exp(block_max - maxima[None])
    totals = jnp.sum(shrink * block_tot, axis=0)
    summed = jnp.sum(shrink[:, :, :, None, :] * sums_recv, axis=0)
    attended_t = summed / totals[:, :, None, :]
    attended = attended_t.reshape(n_head * width, rows).T.astype(jnp.bfloat16)

    own_index = lax.axis_index("cell") * n_head + lax.axis_index("head")
    local_rows = latents.shape[0]
    own_latents = lax.dynamic_slice_in_dim(
        latents, (own_index % (local_rows // rows)) * rows, rows, 0
    )
    projected = jnp.dot(attended, w_out, preferred_element_type=jnp.float32)
    updated = (own_latents.astype(jnp.float32) + projected).astype(jnp.bfloat16)
    widened = updated.astype(jnp.float32)
    normed = (
        widened * lax.rsqrt(jnp.mean(widened * widened, axis=1, keepdims=True) + 1e-05)
    ).astype(jnp.bfloat16)
    chip_normed = lax.all_gather(normed, "head", axis=0, tiled=True)
    hidden = jax.nn.gelu(
        jnp.dot(
            chip_normed,
            lax.all_gather(w_up, "cell", axis=1, tiled=True),
            preferred_element_type=jnp.float32,
        ),
        approximate=True,
    ).astype(jnp.bfloat16)
    mlp_part = jnp.dot(
        hidden,
        lax.all_gather(w_down, "cell", axis=0, tiled=True),
        preferred_element_type=jnp.float32,
    )
    mlp_out = lax.psum_scatter(mlp_part, "head", scatter_dimension=0, tiled=True)
    return (widened + mlp_out).astype(jnp.bfloat16)


def solution(mesh):
    return jax.shard_map(
        body,
        mesh=mesh,
        in_specs=(
            P(("group", "cell"), None),
            P(("group", "cell"), None),
            P(None, "head"),
            P(None, "head"),
            P(None, "head"),
            P(),
            P(None, ("cell", "head")),
            P(("cell", "head"), None),
        ),
        out_specs=P(("group", "cell", "head"), None),
        check_vma=False,
    )
```

```python
import functools

import jax
import jax.numpy as jnp
from jax import lax
from jax.experimental import pallas as pl
from jax.experimental.pallas import tpu as pltpu
from jax.sharding import PartitionSpec as P

HEAD_DIM = 64
LAT_TILE = 512


def attention_kernel(q_ref, k_ref, vt_ref, o_ref, ml_ref):
    factor = HEAD_DIM ** (-0.5)
    for j in range(2):
        cols = slice(j * HEAD_DIM, (j + 1) * HEAD_DIM)
        q = q_ref[:, cols]
        k = k_ref[:, cols]
        scores = (
            lax.dot_general(k, q, (((1,), (1,)), ((), ())), preferred_element_type=jnp.float32)
            * factor
        )
        block_max = jnp.max(scores, axis=0, keepdims=True)
        weights = jnp.exp(scores - block_max)
        block_tot = jnp.sum(weights, axis=0, keepdims=True)
        summed = jnp.dot(
            vt_ref[cols, :], weights.astype(jnp.bfloat16), preferred_element_type=jnp.float32
        )
        o_ref[cols, :] = summed
        ml_ref[0, j : j + 1, :] = block_max
        ml_ref[1, j : j + 1, :] = block_tot


def block_attention(queries, key_rows, value_t):
    lat, width = queries.shape
    cells = key_rows.shape[0]
    pairs = width // (2 * HEAD_DIM)
    tile = min(LAT_TILE, lat)
    return pl.pallas_call(
        attention_kernel,
        grid=(pairs, lat // tile),
        in_specs=[
            pl.BlockSpec((tile, 2 * HEAD_DIM), lambda p, i: (i, p)),
            pl.BlockSpec((cells, 2 * HEAD_DIM), lambda p, i: (0, p)),
            pl.BlockSpec((2 * HEAD_DIM, cells), lambda p, i: (p, 0)),
        ],
        out_specs=[
            pl.BlockSpec((2 * HEAD_DIM, tile), lambda p, i: (p, i)),
            pl.BlockSpec((2, None, 2, tile), lambda p, i: (0, p, 0, i)),
        ],
        out_shape=[
            jax.ShapeDtypeStruct((width, lat), jnp.float32),
            jax.ShapeDtypeStruct((2, pairs, 2, lat), jnp.float32),
        ],
    )(queries, key_rows, value_t)


def body(latents, cells, w_query, w_key, w_value, w_out, w_up, w_down):
    key_rows = jnp.dot(cells, w_key, preferred_element_type=jnp.float32).astype(jnp.bfloat16)
    value_t = jnp.dot(cells, w_value, preferred_element_type=jnp.float32).astype(jnp.bfloat16).T
    local_queries = jnp.dot(latents, w_query, preferred_element_type=jnp.float32).astype(
        jnp.bfloat16
    )
    n_cell = lax.axis_size("cell")
    queries = lax.all_to_all(
        jnp.broadcast_to(local_queries[None], (n_cell,) + local_queries.shape),
        "cell",
        split_axis=0,
        concat_axis=0,
        tiled=True,
    ).reshape(n_cell * local_queries.shape[0], local_queries.shape[1])
    lat, width = queries.shape
    heads_local = width // HEAD_DIM
    n_head = lax.axis_size("head")
    owners = n_cell * n_head
    rows = lat // owners

    sums_t, ml = block_attention(queries, key_rows, value_t)
    ml = ml.reshape(2 * heads_local, lat)
    sums_recv = lax.all_to_all(
        sums_t.astype(jnp.bfloat16), ("cell", "head"), split_axis=1, concat_axis=0, tiled=True
    )
    ml_recv = lax.all_to_all(ml, ("cell", "head"), split_axis=1, concat_axis=0, tiled=True)
    sums_recv = sums_recv.reshape(n_cell, n_head, heads_local, HEAD_DIM, rows).astype(jnp.float32)
    ml_recv = ml_recv.reshape(n_cell, n_head, 2, heads_local, rows)
    block_max = ml_recv[:, :, 0]
    block_tot = ml_recv[:, :, 1]
    maxima = jnp.max(block_max, axis=0)
    shrink = jnp.exp(block_max - maxima[None])
    totals = jnp.sum(shrink * block_tot, axis=0)
    summed = jnp.sum(shrink[:, :, :, None, :] * sums_recv, axis=0)
    attended_t = summed / totals[:, :, None, :]
    attended = attended_t.reshape(n_head * width, rows).T.astype(jnp.bfloat16)

    own_index = lax.axis_index("cell") * n_head + lax.axis_index("head")
    local_rows = latents.shape[0]
    own_latents = lax.dynamic_slice_in_dim(
        latents, (own_index % (local_rows // rows)) * rows, rows, 0
    )
    projected = jnp.dot(attended, w_out, preferred_element_type=jnp.float32)
    updated = (own_latents.astype(jnp.float32) + projected).astype(jnp.bfloat16)
    widened = updated.astype(jnp.float32)
    normed = (
        widened * lax.rsqrt(jnp.mean(widened * widened, axis=1, keepdims=True) + 1e-05)
    ).astype(jnp.bfloat16)
    chip_normed = lax.all_gather(normed, "head", axis=0, tiled=True)
    hidden = jax.nn.gelu(
        lax.dot_general(
            chip_normed,
            lax.all_gather(w_up.T, "cell", axis=0, tiled=True),
            (((1,), (1,)), ((), ())),
            preferred_element_type=jnp.float32,
        ),
        approximate=True,
    ).astype(jnp.bfloat16)
    mlp_part = jnp.dot(
        hidden,
        lax.all_gather(w_down, "cell", axis=0, tiled=True),
        preferred_element_type=jnp.float32,
    )
    mlp_out = lax.psum_scatter(mlp_part, "head", scatter_dimension=0, tiled=True)
    return (widened + mlp_out).astype(jnp.bfloat16)


def solution(mesh):
    return jax.shard_map(
        body,
        mesh=mesh,
        in_specs=(
            P(("group", "cell"), None),
            P(("group", "cell"), None),
            P(None, "head"),
            P(None, "head"),
            P(None, "head"),
            P(),
            P(None, ("cell", "head")),
            P(("cell", "head"), None),
        ),
        out_specs=P(("group", "cell", "head"), None),
        check_vma=False,
    )
```

```python
import functools

import jax
import jax.numpy as jnp
from jax import lax
from jax.experimental import pallas as pl
from jax.experimental.pallas import tpu as pltpu
from jax.sharding import PartitionSpec as P

HEAD_DIM = 64
LAT_TILE = 512


def attention_kernel(q_ref, k_ref, vt_ref, o_ref, ml_ref):
    factor = HEAD_DIM ** (-0.5)
    for j in range(2):
        cols = slice(j * HEAD_DIM, (j + 1) * HEAD_DIM)
        q = q_ref[:, cols]
        k = k_ref[:, cols]
        scores = (
            lax.dot_general(k, q, (((1,), (1,)), ((), ())), preferred_element_type=jnp.float32)
            * factor
        )
        block_max = jnp.max(scores, axis=0, keepdims=True)
        weights = jnp.exp(scores - block_max)
        block_tot = jnp.sum(weights, axis=0, keepdims=True)
        summed = jnp.dot(
            vt_ref[cols, :], weights.astype(jnp.bfloat16), preferred_element_type=jnp.float32
        )
        o_ref[cols, :] = summed
        ml_ref[0, j : j + 1, :] = block_max
        ml_ref[1, j : j + 1, :] = block_tot


def block_attention(queries, key_rows, value_t):
    lat, width = queries.shape
    cells = key_rows.shape[0]
    pairs = width // (2 * HEAD_DIM)
    tile = min(LAT_TILE, lat)
    return pl.pallas_call(
        attention_kernel,
        grid=(pairs, lat // tile),
        in_specs=[
            pl.BlockSpec((tile, 2 * HEAD_DIM), lambda p, i: (i, p)),
            pl.BlockSpec((cells, 2 * HEAD_DIM), lambda p, i: (0, p)),
            pl.BlockSpec((2 * HEAD_DIM, cells), lambda p, i: (p, 0)),
        ],
        out_specs=[
            pl.BlockSpec((2 * HEAD_DIM, tile), lambda p, i: (p, i)),
            pl.BlockSpec((2, None, 2, tile), lambda p, i: (0, p, 0, i)),
        ],
        out_shape=[
            jax.ShapeDtypeStruct((width, lat), jnp.float32),
            jax.ShapeDtypeStruct((2, pairs, 2, lat), jnp.float32),
        ],
    )(queries, key_rows, value_t)


def body(latents, cells, w_query, w_key, w_value, w_out, w_up, w_down):
    key_rows = jnp.dot(cells, w_key, preferred_element_type=jnp.float32).astype(jnp.bfloat16)
    value_t = jnp.dot(cells, w_value, preferred_element_type=jnp.float32).astype(jnp.bfloat16).T
    local_queries = jnp.dot(latents, w_query, preferred_element_type=jnp.float32).astype(
        jnp.bfloat16
    )
    queries = lax.all_gather(local_queries, "cell", axis=0, tiled=True)
    n_cell = lax.axis_size("cell")
    lat, width = queries.shape
    heads_local = width // HEAD_DIM
    n_head = lax.axis_size("head")
    owners = n_cell * n_head
    rows = lat // owners

    sums_t, ml = block_attention(queries, key_rows, value_t)
    ml = ml.reshape(2 * heads_local, lat)
    sums_recv = lax.all_to_all(
        sums_t.astype(jnp.bfloat16), ("cell", "head"), split_axis=1, concat_axis=0, tiled=True
    )
    ml_recv = lax.all_to_all(ml, ("cell", "head"), split_axis=1, concat_axis=0, tiled=True)
    sums_recv = sums_recv.reshape(n_cell, n_head, heads_local, HEAD_DIM, rows).astype(jnp.float32)
    ml_recv = ml_recv.reshape(n_cell, n_head, 2, heads_local, rows)
    block_max = ml_recv[:, :, 0]
    block_tot = ml_recv[:, :, 1]
    maxima = jnp.max(block_max, axis=0)
    shrink = jnp.exp(block_max - maxima[None])
    totals = jnp.sum(shrink * block_tot, axis=0)
    summed = jnp.sum(shrink[:, :, :, None, :] * sums_recv, axis=0)
    attended_t = summed / totals[:, :, None, :]
    attended = attended_t.reshape(n_head * width, rows).T.astype(jnp.bfloat16)

    own_index = lax.axis_index("cell") * n_head + lax.axis_index("head")
    local_rows = latents.shape[0]
    own_latents = lax.dynamic_slice_in_dim(
        latents, (own_index % (local_rows // rows)) * rows, rows, 0
    )
    projected = jnp.dot(attended, w_out, preferred_element_type=jnp.float32)
    updated = (own_latents.astype(jnp.float32) + projected).astype(jnp.bfloat16)
    widened = updated.astype(jnp.float32)
    normed = (
        widened * lax.rsqrt(jnp.mean(widened * widened, axis=1, keepdims=True) + 1e-05)
    ).astype(jnp.bfloat16)
    w_pack = jnp.stack([w_up.T, w_down])
    w_parts = [w_pack]
    for k in range(1, n_cell // 2):
        shift = [(c, (c + 2 * k) % n_cell) for c in range(n_cell)]
        w_parts.append(lax.ppermute(w_pack, "cell", shift))
    w_all = jnp.concatenate(w_parts, axis=1)
    pair = [(c, c ^ 1) for c in range(n_cell)]
    chip_normed = lax.all_gather(normed, "head", axis=0, tiled=True)
    pair_normed = jnp.concatenate([chip_normed, lax.ppermute(chip_normed, "cell", pair)], axis=0)
    hidden = jax.nn.gelu(
        lax.dot_general(
            pair_normed,
            w_all[0],
            (((1,), (1,)), ((), ())),
            preferred_element_type=jnp.float32,
        ),
        approximate=True,
    ).astype(jnp.bfloat16)
    mlp_part = jnp.dot(hidden, w_all[1], preferred_element_type=jnp.float32)
    chip_rows = chip_normed.shape[0]
    mlp_chip = mlp_part[:chip_rows] + lax.ppermute(mlp_part[chip_rows:], "cell", pair)
    mlp_out = lax.psum_scatter(mlp_chip, "head", scatter_dimension=0, tiled=True)
    return (widened + mlp_out).astype(jnp.bfloat16)


def solution(mesh):
    return jax.shard_map(
        body,
        mesh=mesh,
        in_specs=(
            P(("group", "cell"), None),
            P(("group", "cell"), None),
            P(None, "head"),
            P(None, "head"),
            P(None, "head"),
            P(),
            P(None, ("cell", "head")),
            P(("cell", "head"), None),
        ),
        out_specs=P(("group", "cell", "head"), None),
        check_vma=False,
    )
```

```python
import functools

import jax
import jax.numpy as jnp
from jax import lax
from jax.experimental import pallas as pl
from jax.experimental.pallas import tpu as pltpu
from jax.sharding import Mesh
from jax.sharding import PartitionSpec as P

HEAD_DIM = 64
CELL = ("cz", "cx")
LAT_TILE = 512


def attention_kernel(q_ref, k_ref, vt_ref, o_ref, ml_ref):
    factor = HEAD_DIM ** (-0.5)
    for j in range(2):
        cols = slice(j * HEAD_DIM, (j + 1) * HEAD_DIM)
        q = q_ref[:, cols]
        k = k_ref[:, cols]
        scores = (
            lax.dot_general(k, q, (((1,), (1,)), ((), ())), preferred_element_type=jnp.float32)
            * factor
        )
        block_max = jnp.max(scores, axis=0, keepdims=True)
        weights = jnp.exp(scores - block_max)
        block_tot = jnp.sum(weights, axis=0, keepdims=True)
        summed = jnp.dot(
            vt_ref[cols, :], weights.astype(jnp.bfloat16), preferred_element_type=jnp.float32
        )
        o_ref[cols, :] = summed
        ml_ref[0, j : j + 1, :] = block_max
        ml_ref[1, j : j + 1, :] = block_tot


def block_attention(queries, key_rows, value_t):
    lat, width = queries.shape
    cells = key_rows.shape[0]
    pairs = width // (2 * HEAD_DIM)
    tile = min(LAT_TILE, lat)
    return pl.pallas_call(
        attention_kernel,
        grid=(pairs, lat // tile),
        in_specs=[
            pl.BlockSpec((tile, 2 * HEAD_DIM), lambda p, i: (i, p)),
            pl.BlockSpec((cells, 2 * HEAD_DIM), lambda p, i: (0, p)),
            pl.BlockSpec((2 * HEAD_DIM, cells), lambda p, i: (p, 0)),
        ],
        out_specs=[
            pl.BlockSpec((2 * HEAD_DIM, tile), lambda p, i: (p, i)),
            pl.BlockSpec((2, None, 2, tile), lambda p, i: (0, p, 0, i)),
        ],
        out_shape=[
            jax.ShapeDtypeStruct((width, lat), jnp.float32),
            jax.ShapeDtypeStruct((2, pairs, 2, lat), jnp.float32),
        ],
    )(queries, key_rows, value_t)


def body(latents, cells, w_query, w_key, w_value, w_out, w_up, w_down):
    key_rows = jnp.dot(cells, w_key, preferred_element_type=jnp.float32).astype(jnp.bfloat16)
    value_t = jnp.dot(cells, w_value, preferred_element_type=jnp.float32).astype(jnp.bfloat16).T
    local_queries = jnp.dot(latents, w_query, preferred_element_type=jnp.float32).astype(
        jnp.bfloat16
    )
    queries = lax.all_gather(local_queries, CELL, axis=0, tiled=True)
    n_cell = lax.axis_size(CELL)
    lat, width = queries.shape
    heads_local = width // HEAD_DIM
    n_head = lax.axis_size("head")
    owners = n_cell * n_head
    rows = lat // owners

    sums_t, ml = block_attention(queries, key_rows, value_t)
    ml = ml.reshape(2 * heads_local, lat)
    sums_recv = lax.all_to_all(
        sums_t.astype(jnp.bfloat16), CELL + ("head",), split_axis=1, concat_axis=0, tiled=True
    )
    ml_recv = lax.all_to_all(ml, CELL + ("head",), split_axis=1, concat_axis=0, tiled=True)
    sums_recv = sums_recv.reshape(n_cell, n_head, heads_local, HEAD_DIM, rows).astype(jnp.float32)
    ml_recv = ml_recv.reshape(n_cell, n_head, 2, heads_local, rows)
    block_max = ml_recv[:, :, 0]
    block_tot = ml_recv[:, :, 1]
    maxima = jnp.max(block_max, axis=0)
    shrink = jnp.exp(block_max - maxima[None])
    totals = jnp.sum(shrink * block_tot, axis=0)
    summed = jnp.sum(shrink[:, :, :, None, :] * sums_recv, axis=0)
    attended_t = summed / totals[:, :, None, :]
    attended = attended_t.reshape(n_head * width, rows).T.astype(jnp.bfloat16)

    own_index = lax.axis_index(CELL) * n_head + lax.axis_index("head")
    local_rows = latents.shape[0]
    own_latents = lax.dynamic_slice_in_dim(
        latents, (own_index % (local_rows // rows)) * rows, rows, 0
    )
    projected = jnp.dot(attended, w_out, preferred_element_type=jnp.float32)
    updated = (own_latents.astype(jnp.float32) + projected).astype(jnp.bfloat16)
    widened = updated.astype(jnp.float32)
    normed = (
        widened * lax.rsqrt(jnp.mean(widened * widened, axis=1, keepdims=True) + 1e-05)
    ).astype(jnp.bfloat16)
    w_pack = lax.all_gather(jnp.stack([w_up.T, w_down]), "cz", axis=1, tiled=True)
    chip_normed = lax.all_gather(normed, "head", axis=0, tiled=True)
    pair_normed = lax.all_gather(chip_normed, "cx", axis=0, tiled=True)
    hidden = jax.nn.gelu(
        lax.dot_general(
            pair_normed,
            w_pack[0],
            (((1,), (1,)), ((), ())),
            preferred_element_type=jnp.float32,
        ),
        approximate=True,
    ).astype(jnp.bfloat16)
    mlp_part = jnp.dot(hidden, w_pack[1], preferred_element_type=jnp.float32)
    mlp_out = lax.psum_scatter(mlp_part, ("cx", "head"), scatter_dimension=0, tiled=True)
    return (widened + mlp_out).astype(jnp.bfloat16)


def solution(mesh):
    assert tuple(mesh.axis_names) == ("group", "cell", "head")
    sizes = (mesh.shape["group"], mesh.shape["cell"] // 2, 2, mesh.shape["head"])
    split = Mesh(mesh.devices.reshape(sizes), ("group",) + CELL + ("head",))
    return jax.shard_map(
        body,
        mesh=split,
        in_specs=(
            P(("group",) + CELL, None),
            P(("group",) + CELL, None),
            P(None, "head"),
            P(None, "head"),
            P(None, "head"),
            P(),
            P(None, CELL + ("head",)),
            P(CELL + ("head",), None),
        ),
        out_specs=P(("group",) + CELL + ("head",), None),
        check_vma=False,
    )
```

```python
import functools

import jax
import jax.numpy as jnp
from jax import lax
from jax.experimental import pallas as pl
from jax.experimental.pallas import tpu as pltpu
from jax.sharding import Mesh
from jax.sharding import PartitionSpec as P

HEAD_DIM = 64
CELL = ("cz", "cx")
LAT_TILE = 512


def attention_kernel(q_ref, k_ref, vt_ref, o_ref, ml_ref):
    factor = HEAD_DIM ** (-0.5)
    for j in range(2):
        cols = slice(j * HEAD_DIM, (j + 1) * HEAD_DIM)
        q = q_ref[:, cols]
        k = k_ref[:, cols]
        scores = (
            lax.dot_general(k, q, (((1,), (1,)), ((), ())), preferred_element_type=jnp.float32)
            * factor
        )
        block_max = jnp.max(scores, axis=0, keepdims=True)
        weights = jnp.exp(scores - block_max)
        block_tot = jnp.sum(weights, axis=0, keepdims=True)
        summed = jnp.dot(
            vt_ref[cols, :], weights.astype(jnp.bfloat16), preferred_element_type=jnp.float32
        )
        o_ref[cols, :] = summed
        ml_ref[0, j : j + 1, :] = block_max
        ml_ref[1, j : j + 1, :] = block_tot


def block_attention(queries, key_rows, value_t):
    lat, width = queries.shape
    cells = key_rows.shape[0]
    pairs = width // (2 * HEAD_DIM)
    tile = min(LAT_TILE, lat)
    return pl.pallas_call(
        attention_kernel,
        grid=(pairs, lat // tile),
        in_specs=[
            pl.BlockSpec((tile, 2 * HEAD_DIM), lambda p, i: (i, p)),
            pl.BlockSpec((cells, 2 * HEAD_DIM), lambda p, i: (0, p)),
            pl.BlockSpec((2 * HEAD_DIM, cells), lambda p, i: (p, 0)),
        ],
        out_specs=[
            pl.BlockSpec((2 * HEAD_DIM, tile), lambda p, i: (p, i)),
            pl.BlockSpec((2, None, 2, tile), lambda p, i: (0, p, 0, i)),
        ],
        out_shape=[
            jax.ShapeDtypeStruct((width, lat), jnp.float32),
            jax.ShapeDtypeStruct((2, pairs, 2, lat), jnp.float32),
        ],
    )(queries, key_rows, value_t)


def body(latents, cells, w_query, w_key, w_value, w_out, w_up, w_down):
    key_rows = jnp.dot(cells, w_key, preferred_element_type=jnp.float32).astype(jnp.bfloat16)
    value_t = jnp.dot(cells, w_value, preferred_element_type=jnp.float32).astype(jnp.bfloat16).T
    local_queries = jnp.dot(latents, w_query, preferred_element_type=jnp.float32).astype(
        jnp.bfloat16
    )
    queries = lax.all_gather(local_queries, CELL, axis=0, tiled=True)
    n_cell = lax.axis_size(CELL)
    lat, width = queries.shape
    heads_local = width // HEAD_DIM
    n_head = lax.axis_size("head")
    owners = n_cell * n_head
    rows = lat // owners

    sums_t, ml = block_attention(queries, key_rows, value_t)
    ml = ml.reshape(2 * heads_local, lat)
    sums_recv = lax.all_to_all(
        sums_t.astype(jnp.bfloat16), CELL + ("head",), split_axis=1, concat_axis=0, tiled=True
    )
    ml_recv = lax.all_to_all(ml, CELL + ("head",), split_axis=1, concat_axis=0, tiled=True)
    sums_recv = sums_recv.reshape(n_cell, n_head, heads_local, HEAD_DIM, rows).astype(jnp.float32)
    ml_recv = ml_recv.reshape(n_cell, n_head, 2, heads_local, rows)
    block_max = ml_recv[:, :, 0]
    block_tot = ml_recv[:, :, 1]
    maxima = jnp.max(block_max, axis=0)
    shrink = jnp.exp(block_max - maxima[None])
    totals = jnp.sum(shrink * block_tot, axis=0)
    summed = jnp.sum(shrink[:, :, :, None, :] * sums_recv, axis=0)
    attended_t = summed / totals[:, :, None, :]
    attended = attended_t.reshape(n_head * width, rows).T.astype(jnp.bfloat16)

    own_index = lax.axis_index(CELL) * n_head + lax.axis_index("head")
    local_rows = latents.shape[0]
    own_latents = lax.dynamic_slice_in_dim(
        latents, (own_index % (local_rows // rows)) * rows, rows, 0
    )
    projected = jnp.dot(attended, w_out, preferred_element_type=jnp.float32)
    updated = (own_latents.astype(jnp.float32) + projected).astype(jnp.bfloat16)
    widened = updated.astype(jnp.float32)
    normed = (
        widened * lax.rsqrt(jnp.mean(widened * widened, axis=1, keepdims=True) + 1e-05)
    ).astype(jnp.bfloat16)
    w_pack = lax.all_gather(jnp.stack([w_up.T, w_down]), "cz", axis=1, tiled=True)
    chip_normed = lax.all_gather(normed, "head", axis=0, tiled=True)
    swap = [(0, 1), (1, 0)]
    pair_normed = jnp.concatenate([chip_normed, lax.ppermute(chip_normed, "cx", swap)], axis=0)
    hidden = jax.nn.gelu(
        lax.dot_general(
            pair_normed,
            w_pack[0],
            (((1,), (1,)), ((), ())),
            preferred_element_type=jnp.float32,
        ),
        approximate=True,
    ).astype(jnp.bfloat16)
    mlp_part = jnp.dot(hidden, w_pack[1], preferred_element_type=jnp.float32)
    chip_rows = chip_normed.shape[0]
    mlp_chip = mlp_part[:chip_rows] + lax.ppermute(mlp_part[chip_rows:], "cx", swap)
    mlp_out = lax.psum_scatter(mlp_chip, "head", scatter_dimension=0, tiled=True)
    return (widened + mlp_out).astype(jnp.bfloat16)


def solution(mesh):
    assert tuple(mesh.axis_names) == ("group", "cell", "head")
    sizes = (mesh.shape["group"], mesh.shape["cell"] // 2, 2, mesh.shape["head"])
    split = Mesh(mesh.devices.reshape(sizes), ("group",) + CELL + ("head",))
    return jax.shard_map(
        body,
        mesh=split,
        in_specs=(
            P(("group",) + CELL, None),
            P(("group",) + CELL, None),
            P(None, "head"),
            P(None, "head"),
            P(None, "head"),
            P(),
            P(None, CELL + ("head",)),
            P(CELL + ("head",), None),
        ),
        out_specs=P(("group",) + CELL + ("head",), None),
        check_vma=False,
    )
```

```python
import functools

import jax
import jax.numpy as jnp
from jax import lax
from jax.experimental import pallas as pl
from jax.experimental.pallas import tpu as pltpu
from jax.sharding import Mesh
from jax.sharding import PartitionSpec as P

HEAD_DIM = 64
CELL = ("cz", "cx")
LAT_TILE = 512


def attention_kernel(q_ref, k_ref, vt_ref, o_ref, ml_ref):
    factor = HEAD_DIM ** (-0.5)
    for j in range(2):
        cols = slice(j * HEAD_DIM, (j + 1) * HEAD_DIM)
        q = q_ref[:, cols]
        k = k_ref[:, cols]
        scores = (
            lax.dot_general(k, q, (((1,), (1,)), ((), ())), preferred_element_type=jnp.float32)
            * factor
        )
        block_max = jnp.max(scores, axis=0, keepdims=True)
        weights = jnp.exp(scores - block_max)
        block_tot = jnp.sum(weights, axis=0, keepdims=True)
        summed = jnp.dot(
            vt_ref[cols, :], weights.astype(jnp.bfloat16), preferred_element_type=jnp.float32
        )
        o_ref[cols, :] = summed
        ml_ref[0, j : j + 1, :] = block_max
        ml_ref[1, j : j + 1, :] = block_tot


def block_attention(queries, key_rows, value_t):
    lat, width = queries.shape
    cells = key_rows.shape[0]
    pairs = width // (2 * HEAD_DIM)
    tile = min(LAT_TILE, lat)
    return pl.pallas_call(
        attention_kernel,
        grid=(pairs, lat // tile),
        in_specs=[
            pl.BlockSpec((tile, 2 * HEAD_DIM), lambda p, i: (i, p)),
            pl.BlockSpec((cells, 2 * HEAD_DIM), lambda p, i: (0, p)),
            pl.BlockSpec((2 * HEAD_DIM, cells), lambda p, i: (p, 0)),
        ],
        out_specs=[
            pl.BlockSpec((2 * HEAD_DIM, tile), lambda p, i: (p, i)),
            pl.BlockSpec((2, None, 2, tile), lambda p, i: (0, p, 0, i)),
        ],
        out_shape=[
            jax.ShapeDtypeStruct((width, lat), jnp.float32),
            jax.ShapeDtypeStruct((2, pairs, 2, lat), jnp.float32),
        ],
    )(queries, key_rows, value_t)


def body(latents, cells, w_query, w_key, w_value, w_out, w_up, w_down):
    key_rows = jnp.dot(cells, w_key, preferred_element_type=jnp.float32).astype(jnp.bfloat16)
    value_t = jnp.dot(cells, w_value, preferred_element_type=jnp.float32).astype(jnp.bfloat16).T
    local_queries = jnp.dot(latents, w_query, preferred_element_type=jnp.float32).astype(
        jnp.bfloat16
    )
    n_cell = lax.axis_size(CELL)
    n_head = lax.axis_size("head")
    lat = n_cell * local_queries.shape[0]
    width = local_queries.shape[1]
    heads_local = width // HEAD_DIM
    owners = n_cell * n_head
    rows = lat // owners
    half = width // 2
    sums_parts = []
    ml_parts = []
    for part in range(2):
        cols = slice(part * half, (part + 1) * half)
        queries = lax.all_gather(local_queries[:, cols], CELL, axis=0, tiled=True)
        sums_t, ml = block_attention(queries, key_rows[:, cols], value_t[cols])
        sums_parts.append(
            lax.all_to_all(
                sums_t.astype(jnp.bfloat16), CELL + ("head",), split_axis=1, concat_axis=0, tiled=True
            ).reshape(owners, half, rows)
        )
        ml_parts.append(ml.reshape(2, heads_local // 2, lat))
    ml = jnp.concatenate(ml_parts, axis=1).reshape(2 * heads_local, lat)
    sums_recv = jnp.concatenate(sums_parts, axis=1)
    ml_recv = lax.all_to_all(ml, CELL + ("head",), split_axis=1, concat_axis=0, tiled=True)
    sums_recv = sums_recv.reshape(n_cell, n_head, heads_local, HEAD_DIM, rows).astype(jnp.float32)
    ml_recv = ml_recv.reshape(n_cell, n_head, 2, heads_local, rows)
    block_max = ml_recv[:, :, 0]
    block_tot = ml_recv[:, :, 1]
    maxima = jnp.max(block_max, axis=0)
    shrink = jnp.exp(block_max - maxima[None])
    totals = jnp.sum(shrink * block_tot, axis=0)
    summed = jnp.sum(shrink[:, :, :, None, :] * sums_recv, axis=0)
    attended_t = summed / totals[:, :, None, :]
    attended = attended_t.reshape(n_head * width, rows).T.astype(jnp.bfloat16)

    own_index = lax.axis_index(CELL) * n_head + lax.axis_index("head")
    local_rows = latents.shape[0]
    own_latents = lax.dynamic_slice_in_dim(
        latents, (own_index % (local_rows // rows)) * rows, rows, 0
    )
    projected = jnp.dot(attended, w_out, preferred_element_type=jnp.float32)
    updated = (own_latents.astype(jnp.float32) + projected).astype(jnp.bfloat16)
    widened = updated.astype(jnp.float32)
    normed = (
        widened * lax.rsqrt(jnp.mean(widened * widened, axis=1, keepdims=True) + 1e-05)
    ).astype(jnp.bfloat16)
    w_pack = lax.all_gather(jnp.stack([w_up.T, w_down]), "cz", axis=1, tiled=True)
    chip_normed = lax.all_gather(normed, "head", axis=0, tiled=True)
    swap = [(0, 1), (1, 0)]
    pair_normed = jnp.concatenate([chip_normed, lax.ppermute(chip_normed, "cx", swap)], axis=0)
    hidden = jax.nn.gelu(
        lax.dot_general(
            pair_normed,
            w_pack[0],
            (((1,), (1,)), ((), ())),
            preferred_element_type=jnp.float32,
        ),
        approximate=True,
    ).astype(jnp.bfloat16)
    mlp_part = jnp.dot(hidden, w_pack[1], preferred_element_type=jnp.float32)
    chip_rows = chip_normed.shape[0]
    back = lax.ppermute(mlp_part[chip_rows:].astype(jnp.bfloat16), "cx", swap)
    mlp_chip = mlp_part[:chip_rows] + back.astype(jnp.float32)
    mlp_out = lax.psum_scatter(mlp_chip, "head", scatter_dimension=0, tiled=True)
    return (widened + mlp_out).astype(jnp.bfloat16)


def solution(mesh):
    assert tuple(mesh.axis_names) == ("group", "cell", "head")
    sizes = (mesh.shape["group"], mesh.shape["cell"] // 2, 2, mesh.shape["head"])
    split = Mesh(mesh.devices.reshape(sizes), ("group",) + CELL + ("head",))
    return jax.shard_map(
        body,
        mesh=split,
        in_specs=(
            P(("group",) + CELL, None),
            P(("group",) + CELL, None),
            P(None, "head"),
            P(None, "head"),
            P(None, "head"),
            P(),
            P(None, CELL + ("head",)),
            P(CELL + ("head",), None),
        ),
        out_specs=P(("group",) + CELL + ("head",), None),
        check_vma=False,
    )
```
